512 devices in a mesh: aux: 16 (over z, x_lo), ao: 32 (over y, x_hi, core).
Axes of the slice: x: 4 (x_hi: 2, x_lo: 2; x = x_hi * 2 + x_lo), y: 8, z: 8, core: 2. Of those that a mesh axis runs over, the one named last changes fastest.
Arguments:
- soc_ints: bfloat16 [2048, 3, 16, 8192], P('aux', None, None, 'ao'), may hold values from -6 to 6
- cou_ints: bfloat16 [2048, 16, 8192], P('aux', None, 'ao'), may hold values from -6 to 6
- coef_t: bfloat16 [16, 8192], P(None, 'ao'), may hold values from -0.0625 to 0.0625
- active_rdm: float32 [16, 16], replicated, may hold values from -3 to 3
- spin_dens: bfloat16 [320, 256], P('ao'), may hold values from -6 to 6
- pair_list: int32 [320, 2], replicated, may hold values from 0 to 23
- owner_map: int32 [320], P('ao'), may hold values from 0 to 319, each once
- state_count: int32 [24], replicated, may hold values from 8 to 16, as said below
Outputs:
- soc_elems: float32 [3, 320], P(None, 'ao')
The draws below stay inside these ranges and needn't reach their ends.
Inputs may be any that keep to these rules, and one draw needn't show every extreme that they name: `state_count`: each state's count of live active orbitals; some state has all 16. `owner_map`: every pair appears in exactly one slot.
All inputs are finite; a program needn't handle non-finite values.
Results may differ from the reference program's by a relative error of at most 0.0003.
Values may be sent and summed in bfloat16 or wider, within the bound.
No kernel may reach another device: no remote copies, remote signals or barrier semaphores. Data moves between devices by JAX's collectives and lax.ppermute only.
A program may use at most 64 MiB of HBM per device.

```python
import jax
import jax.numpy as jnp
from jax import lax

NAO = 8192
NACT = 16
NSTATE = 24
NAUX = 2048
NPAIR = 320


def draw_state_count(key, part):
    counts = jax.random.randint(jax.random.fold_in(key, 11), (NSTATE,), NACT // 2, NACT + 1)
    chosen = jax.random.randint(jax.random.fold_in(key, 12), (), 0, NSTATE)
    return jnp.where(jnp.arange(NSTATE) == chosen, NACT, counts).astype(jnp.int32)


def plant(array, key, least, largest):
    place = [jax.random.randint(jax.random.fold_in(key, axis), (), 0, length) for axis, length in enumerate(array.shape)]
    main_axis = array.shape.index(max(array.shape))
    next_to = place[:main_axis] + [(place[main_axis] + 1) % array.shape[main_axis]] + place[main_axis + 1:]
    return array.at[tuple(place)].set(least).at[tuple(next_to)].set(largest)


def level_of(stream_key, dims, shards, least, largest):
    def one(dim, shards_of):
        heights = jax.random.uniform(jax.random.fold_in(jax.random.fold_in(stream_key, 6), dim), (shards_of,), jnp.float32, least / len(shards), largest / len(shards))
        return jnp.repeat(jnp.exp(heights), dims[dim] // shards_of).reshape((-1,) + (1,) * (len(dims) - dim - 1))

    level = one(*shards[0])
    for cut in shards[1:]:
        level = level * one(*cut)
    return level


def scatter_about(stream_key, shape, scale, most, cuts=(), kind=jnp.bfloat16):
    array = jax.random.normal(stream_key, shape, jnp.float32) * scale
    if len(cuts) > 0:
        array = level_of(stream_key, shape, cuts, -0.22, 0.18) * array
    return jnp.clip(array, min=-most, max=most).astype(kind)


def setup_inputs(seed: int = 0) -> dict:
    seeds = jax.random.split(jax.random.key(seed), 9)
    soc_ints = scatter_about(seeds[0], (NAUX, 3, NACT, NAO), 1.0, 6.0, ((0, 16), (3, 32)))
    cou_ints = scatter_about(seeds[1], (NAUX, NACT, NAO), 1.0, 6.0, ((0, 16), (2, 32)))
    coef_t = scatter_about(seeds[2], (NACT, NAO), NAO ** -0.5, 0.0625, ((1, 32),))
    active_rdm = scatter_about(seeds[3], (NACT, NACT), 0.5, 3.0, (), jnp.float32)
    spin_dens = scatter_about(seeds[4], (NPAIR, NACT * NACT), 1.0, 6.0, ((0, 32),))
    pair_list = plant(jax.random.randint(seeds[5], (NPAIR, 2), 0, NSTATE), jax.random.fold_in(seeds[5], 1), 0, NSTATE - 1).astype(jnp.int32)
    owner_map = jax.random.permutation(seeds[6], NPAIR).astype(jnp.int32)
    state_count = draw_state_count(jax.random.fold_in(seeds[8], 71), 0)
    return dict(soc_ints=soc_ints, cou_ints=cou_ints, coef_t=coef_t, active_rdm=active_rdm, spin_dens=spin_dens, pair_list=pair_list, owner_map=owner_map, state_count=state_count)


def mean_field(soc_rows, cou_rows, active_rdm, scale):
    count = soc_rows.shape[0]
    width = active_rdm.shape[0]
    high = lax.Precision.HIGHEST
    fitted = jnp.dot(cou_rows, active_rdm.reshape(-1), precision=high)
    direct = jnp.einsum('p,pxk->xk', fitted, soc_rows, precision=high)
    folded = jnp.einsum('vw,pwu->pvu', active_rdm, cou_rows.reshape(count, width, width), precision=high)
    crossed = jnp.einsum('pxtv,pvu->xtu', soc_rows.reshape(count, 3, width, width), folded, precision=high)
    return (direct - 1.5 * crossed.reshape(3, width * width)) * scale

def reference(soc_ints, cou_ints, coef_t, active_rdm, spin_dens, pair_list, owner_map, state_count):
    width = NACT
    cells = width * width
    soc_mo = jnp.dot(soc_ints.reshape(-1, NAO), coef_t.T, preferred_element_type=jnp.float32).reshape(NAUX, 3, cells)
    cou_mo = jnp.dot(cou_ints.reshape(-1, NAO), coef_t.T, preferred_element_type=jnp.float32).reshape(NAUX, cells)
    scale = 1.0 / (8.0 * jnp.sqrt(jnp.float32(NAUX)))
    field = mean_field(soc_mo, cou_mo, active_rdm, scale)
    bra_count = state_count[pair_list[:, 0]]
    ket_count = state_count[pair_list[:, 1]]
    live = jnp.minimum(bra_count, ket_count)
    cell = jnp.arange(cells, dtype=jnp.int32)
    inside = (cell[None, :] // width < live[:, None]) & (cell[None, :] % width < live[:, None])
    dens = jnp.where(inside, spin_dens.astype(jnp.float32), jnp.float32(0.0))
    pair_val = jnp.dot(field, dens.T, precision=lax.Precision.HIGHEST) / width
    return jnp.take(pair_val, owner_map, axis=1)
```

```python
import jax
import jax.numpy as jnp
import numpy as np
from jax import lax
from jax.sharding import Mesh
from jax.sharding import PartitionSpec as P

AUX = ("z", "xlo")
AO = ("y", "xhi", "core")
HIGH = lax.Precision.HIGHEST


def butterfly_sum(value, rounds):
    for axis, size in rounds:
        step = 1
        while step < size:
            pairs = [(i, i ^ step) for i in range(size)]
            value = value + lax.ppermute(value, axis, pairs)
            step *= 2
    return value


def butterfly_gather(value, rounds):
    for axis, size in rounds:
        step = 1
        while step < size:
            pairs = [(i, i ^ step) for i in range(size)]
            value = jnp.concatenate([value, lax.ppermute(value, axis, pairs)], axis=0)
            step *= 2
    return value


AO_ROUNDS = (("core", 2), ("xhi", 2), ("y", 8))
AUX_ROUNDS = (("xlo", 2), ("z", 8))


def on_device(soc_ints, cou_ints, coef_t, active_rdm, spin_dens, pair_list, owner_map, state_count):
    width = coef_t.shape[0]
    cells = width * width
    rows = soc_ints.shape[0]
    n_aux = lax.axis_size("z") * lax.axis_size("xlo")
    scale = 1.0 / (8.0 * jnp.sqrt(jnp.float32(rows * n_aux)))

    cou_part = jnp.einsum(
        "ptn,un->ptu", cou_ints, coef_t, preferred_element_type=jnp.float32
    ).reshape(rows, cells)
    cou_mo = butterfly_sum(cou_part, AO_ROUNDS)

    soc_part = jnp.einsum(
        "pxtn,un->xtpu", soc_ints, coef_t, preferred_element_type=jnp.float32
    ).reshape(3 * width, rows * width)

    fitted = jnp.dot(cou_mo, active_rdm.reshape(-1), precision=HIGH)
    folded = jnp.einsum("vw,pwu->pvu", active_rdm, cou_mo.reshape(rows, width, width), precision=HIGH)
    eye = jnp.eye(width, dtype=jnp.float32)
    weight = fitted[:, None, None] * eye[None] - 1.5 * folded
    field_part = jnp.dot(soc_part, weight.reshape(rows * width, width), precision=HIGH)
    field_part = (field_part * scale).reshape(3, cells)
    field = butterfly_sum(field_part, AO_ROUNDS + AUX_ROUNDS)

    me = (lax.axis_index("y") * 4 + lax.axis_index("xhi") * 2 + lax.axis_index("core")).astype(jnp.int32)
    block = spin_dens.shape[0]
    every_dens = butterfly_gather(spin_dens, AO_ROUNDS)
    where = (owner_map // block) ^ me
    picked = jnp.take(every_dens, where * block + owner_map % block, axis=0)

    bra = jnp.take(state_count, jnp.take(pair_list[:, 0], owner_map, axis=0), axis=0)
    ket = jnp.take(state_count, jnp.take(pair_list[:, 1], owner_map, axis=0), axis=0)
    live = jnp.minimum(bra, ket)
    cell = jnp.arange(cells, dtype=jnp.int32)
    inside = (cell[None, :] // width < live[:, None]) & (cell[None, :] % width < live[:, None])
    dens = jnp.where(inside, picked.astype(jnp.float32), jnp.float32(0.0))
    return jnp.dot(field, dens.T, precision=HIGH) / width


def solution(mesh):
    devices = np.asarray(mesh.devices).reshape(8, 2, 8, 2, 2)
    fine = Mesh(devices, AUX + AO)
    return jax.shard_map(
        on_device,
        mesh=fine,
        in_specs=(
            P(AUX, None, None, AO),
            P(AUX, None, AO),
            P(None, AO),
            P(),
            P(AO, None),
            P(),
            P(AO),
            P(),
        ),
        out_specs=P(None, AO),
        check_vma=False,
    )
```

```python
import jax
import jax.numpy as jnp
import numpy as np
from jax import lax
from jax.sharding import Mesh
from jax.sharding import PartitionSpec as P

AUX = ("z", "xlo")
AO = ("y", "xhi", "core")
HIGH = lax.Precision.HIGHEST
AO_ROUNDS = (("core", 2), ("xhi", 2), ("y", 8))
AUX_ROUNDS = (("xlo", 2), ("z", 8))


def partners(size, step):
    return [(i, i ^ step) for i in range(size)]


def butterfly_sum(value, rounds):
    for axis, size in rounds:
        step = 1
        while step < size:
            value = value + lax.ppermute(value, axis, partners(size, step))
            step *= 2
    return value


def butterfly_sum_gather(total, blocks, rounds):
    for axis, size in rounds:
        step = 1
        while step < size:
            pairs = partners(size, step)
            total = total + lax.ppermute(total, axis, pairs)
            blocks = jnp.concatenate([blocks, lax.ppermute(blocks, axis, pairs)], axis=0)
            total, blocks = lax.optimization_barrier((total, blocks))
            step *= 2
    return total, blocks


def on_device(soc_ints, cou_ints, coef_t, active_rdm, spin_dens, pair_list, owner_map, state_count):
    width = coef_t.shape[0]
    cells = width * width
    rows = soc_ints.shape[0]
    n_aux = lax.axis_size("z") * lax.axis_size("xlo")
    scale = 1.0 / (8.0 * jnp.sqrt(jnp.float32(rows * n_aux)))

    cou_part = jnp.einsum("un,ptn->upt", coef_t, cou_ints, preferred_element_type=jnp.float32)
    fitted = jnp.einsum("upt,tu->p", cou_part, active_rdm, precision=HIGH)
    folded = jnp.einsum("upw,vw->uvp", cou_part, active_rdm, precision=HIGH)
    eye = jnp.eye(width, dtype=jnp.float32)
    weight = (eye[:, :, None] * fitted[None, None, :] - 1.5 * folded).reshape(width, width * rows)
    weight, every_dens = butterfly_sum_gather(weight, spin_dens, AO_ROUNDS)

    soc_part = jnp.einsum(
        "vn,pkn->vpk", coef_t, soc_ints.reshape(rows, 3 * width, -1), preferred_element_type=jnp.float32
    ).reshape(width * rows, 3 * width)
    field_part = jnp.dot(weight, soc_part, precision=HIGH) * scale
    field = butterfly_sum(field_part, AO_ROUNDS + AUX_ROUNDS)

    me = (lax.axis_index("y") * 4 + lax.axis_index("xhi") * 2 + lax.axis_index("core")).astype(jnp.int32)
    block = spin_dens.shape[0]
    where = (owner_map // block) ^ me
    picked = jnp.take(every_dens, where * block + owner_map % block, axis=0)

    bra = jnp.take(state_count, jnp.take(pair_list[:, 0], owner_map, axis=0), axis=0)
    ket = jnp.take(state_count, jnp.take(pair_list[:, 1], owner_map, axis=0), axis=0)
    live = jnp.minimum(bra, ket)
    cell = jnp.arange(cells, dtype=jnp.int32)
    inside = (cell[None, :] // width < live[:, None]) & (cell[None, :] % width < live[:, None])
    dens = jnp.where(inside, picked.astype(jnp.float32), jnp.float32(0.0))
    return jnp.einsum(
        "uxt,stu->xs", field.reshape(width, 3, width), dens.reshape(-1, width, width), precision=HIGH
    ) / width


def solution(mesh):
    devices = np.asarray(mesh.devices).reshape(8, 2, 8, 2, 2)
    fine = Mesh(devices, AUX + AO)
    return jax.shard_map(
        on_device,
        mesh=fine,
        in_specs=(
            P(AUX, None, None, AO),
            P(AUX, None, AO),
            P(None, AO),
            P(),
            P(AO, None),
            P(),
            P(AO),
            P(),
        ),
        out_specs=P(None, AO),
        check_vma=False,
    )
```

```python
import jax
import jax.numpy as jnp
import numpy as np
from jax import lax
from jax.sharding import Mesh
from jax.sharding import PartitionSpec as P

AUX = ("z", "xlo")
AO = ("y", "xhi", "core")
HIGH = lax.Precision.HIGHEST
AO_ROUNDS = (("core", 2), ("xhi", 2), ("y", 8))
AUX_ROUNDS = (("xlo", 2), ("z", 8))


def partners(size, step):
    return [(i, i ^ step) for i in range(size)]


def butterfly_sum(value, rounds):
    for axis, size in rounds:
        step = 1
        while step < size:
            value = value + lax.ppermute(value, axis, partners(size, step))
            step *= 2
    return value


def butterfly_sum_gather(total, blocks, rounds):
    count = total.shape[0]
    for axis, size in rounds:
        step = 1
        while step < size:
            got = lax.ppermute(jnp.concatenate([total, blocks], axis=0), axis, partners(size, step))
            total = total + got[:count]
            blocks = jnp.concatenate([blocks, got[count:]], axis=0)
            step *= 2
    return total, blocks


def on_device(soc_ints, cou_ints, coef_t, active_rdm, spin_dens, pair_list, owner_map, state_count):
    width = coef_t.shape[0]
    cells = width * width
    rows = soc_ints.shape[0]
    n_aux = lax.axis_size("z") * lax.axis_size("xlo")
    scale = 1.0 / (8.0 * jnp.sqrt(jnp.float32(rows * n_aux)))

    cou_part = jnp.einsum("un,ptn->upt", coef_t, cou_ints, preferred_element_type=jnp.float32)
    fitted = jnp.einsum("upt,tu->p", cou_part, active_rdm, precision=HIGH)
    folded = jnp.einsum("upw,vw->uvp", cou_part, active_rdm, precision=HIGH)
    eye = jnp.eye(width, dtype=jnp.float32)
    weight = (eye[:, :, None] * fitted[None, None, :] - 1.5 * folded).reshape(width, width * rows)
    block = spin_dens.shape[0]
    slot = -(-block // width) * width
    lane = weight.shape[1]
    own_dens = jnp.pad(spin_dens.astype(jnp.float32), ((0, slot - block), (0, 0))).reshape(-1, lane)
    weight, every_dens = butterfly_sum_gather(weight, own_dens, AO_ROUNDS)
    every_dens = every_dens.reshape(-1, cells)

    soc_part = jnp.einsum(
        "vn,pkn->vpk", coef_t, soc_ints.reshape(rows, 3 * width, -1), preferred_element_type=jnp.float32
    ).reshape(width * rows, 3 * width)
    field_part = jnp.dot(weight, soc_part, precision=HIGH) * scale
    field = butterfly_sum(field_part, AO_ROUNDS + AUX_ROUNDS)

    me = (lax.axis_index("y") * 4 + lax.axis_index("xhi") * 2 + lax.axis_index("core")).astype(jnp.int32)
    where = (owner_map // block) ^ me
    picked = jnp.take(every_dens, where * slot + owner_map % block, axis=0)

    bra = jnp.take(state_count, jnp.take(pair_list[:, 0], owner_map, axis=0), axis=0)
    ket = jnp.take(state_count, jnp.take(pair_list[:, 1], owner_map, axis=0), axis=0)
    live = jnp.minimum(bra, ket)
    cell = jnp.arange(cells, dtype=jnp.int32)
    inside = (cell[None, :] // width < live[:, None]) & (cell[None, :] % width < live[:, None])
    dens = jnp.where(inside, picked, jnp.float32(0.0))
    return jnp.einsum(
        "uxt,stu->xs", field.reshape(width, 3, width), dens.reshape(-1, width, width), precision=HIGH
    ) / width


def solution(mesh):
    devices = np.asarray(mesh.devices).reshape(8, 2, 8, 2, 2)
    fine = Mesh(devices, AUX + AO)
    return jax.shard_map(
        on_device,
        mesh=fine,
        in_specs=(
            P(AUX, None, None, AO),
            P(AUX, None, AO),
            P(None, AO),
            P(),
            P(AO, None),
            P(),
            P(AO),
            P(),
        ),
        out_specs=P(None, AO),
        check_vma=False,
    )
```

```python
import jax
import jax.numpy as jnp
import numpy as np
from jax import lax
from jax.sharding import Mesh
from jax.sharding import PartitionSpec as P

AUX = ("z", "xlo")
AO = ("y", "xhi", "core")
HIGH = lax.Precision.HIGHEST
AO_ROUNDS = (("core", 2), ("xhi", 2), ("y", 8))
AUX_ROUNDS = (("xlo", 2), ("z", 8))


def partners(size, step):
    return [(i, i ^ step) for i in range(size)]


def butterfly_sum(value, rounds):
    for axis, size in rounds:
        step = 1
        while step < size:
            value = value + lax.ppermute(value, axis, partners(size, step))
            step *= 2
    return value


def butterfly_sum_gather(total, blocks, rounds):
    count = total.shape[0]
    for axis, size in rounds:
        step = 1
        while step < size:
            high = lax.reduce_precision(total, exponent_bits=8, mantissa_bits=7)
            low = total - high
            message = jnp.concatenate(
                [high.astype(jnp.bfloat16), low.astype(jnp.bfloat16), blocks], axis=0
            )
            got = lax.ppermute(message, axis, partners(size, step))
            sent = got[:count].astype(jnp.float32) + got[count : 2 * count].astype(jnp.float32)
            total = total + sent
            blocks = jnp.concatenate([blocks, got[2 * count :]], axis=0)
            step *= 2
    return total, blocks


def on_device(soc_ints, cou_ints, coef_t, active_rdm, spin_dens, pair_list, owner_map, state_count):
    width = coef_t.shape[0]
    cells = width * width
    rows = soc_ints.shape[0]
    n_aux = lax.axis_size("z") * lax.axis_size("xlo")
    scale = 1.0 / (8.0 * jnp.sqrt(jnp.float32(rows * n_aux)))

    cou_part = jnp.einsum("un,ptn->upt", coef_t, cou_ints, preferred_element_type=jnp.float32)
    fitted = jnp.einsum("upt,tu->p", cou_part, active_rdm, precision=HIGH)
    folded = jnp.einsum("upw,vw->uvp", cou_part, active_rdm, precision=HIGH)
    eye = jnp.eye(width, dtype=jnp.float32)
    weight = (eye[:, :, None] * fitted[None, None, :] - 1.5 * folded).reshape(width, width * rows)
    block = spin_dens.shape[0]
    slot = -(-block // width) * width
    lane = weight.shape[1]
    own_dens = jnp.pad(spin_dens, ((0, slot - block), (0, 0))).reshape(-1, lane)
    weight, every_dens = butterfly_sum_gather(weight, own_dens, AO_ROUNDS)
    every_dens = every_dens.reshape(-1, cells)

    soc_part = jnp.einsum(
        "vn,pkn->vpk", coef_t, soc_ints.reshape(rows, 3 * width, -1), preferred_element_type=jnp.float32
    ).reshape(width * rows, 3 * width)
    field_part = jnp.dot(weight, soc_part, precision=HIGH) * scale
    field = butterfly_sum(field_part, AO_ROUNDS + AUX_ROUNDS)

    me = (lax.axis_index("y") * 4 + lax.axis_index("xhi") * 2 + lax.axis_index("core")).astype(jnp.int32)
    where = (owner_map // block) ^ me
    picked = jnp.take(every_dens, where * slot + owner_map % block, axis=0)

    bra = jnp.take(state_count, jnp.take(pair_list[:, 0], owner_map, axis=0), axis=0)
    ket = jnp.take(state_count, jnp.take(pair_list[:, 1], owner_map, axis=0), axis=0)
    live = jnp.minimum(bra, ket)
    cell = jnp.arange(cells, dtype=jnp.int32)
    inside = (cell[None, :] // width < live[:, None]) & (cell[None, :] % width < live[:, None])
    dens = jnp.where(inside, picked.astype(jnp.float32), jnp.float32(0.0))
    return jnp.einsum(
        "uxt,stu->xs", field.reshape(width, 3, width), dens.reshape(-1, width, width), precision=HIGH
    ) / width


def solution(mesh):
    devices = np.asarray(mesh.devices).reshape(8, 2, 8, 2, 2)
    fine = Mesh(devices, AUX + AO)
    return jax.shard_map(
        on_device,
        mesh=fine,
        in_specs=(
            P(AUX, None, None, AO),
            P(AUX, None, AO),
            P(None, AO),
            P(),
            P(AO, None),
            P(),
            P(AO),
            P(),
        ),
        out_specs=P(None, AO),
        check_vma=False,
    )
```

```python
import jax
import jax.numpy as jnp
import numpy as np
from jax import lax
from jax.sharding import Mesh
from jax.sharding import PartitionSpec as P

AUX = ("z", "xlo")
AO = ("y", "xhi", "core")
HIGH = lax.Precision.HIGHEST
AO_ROUNDS = (("core", 2), ("xhi", 2), ("y", 8))
AUX_ROUNDS = (("xlo", 2), ("z", 8))


def partners(size, step):
    return [(i, i ^ step) for i in range(size)]


def butterfly_sum(value, rounds):
    for axis, size in rounds:
        step = 1
        while step < size:
            value = value + lax.ppermute(value, axis, partners(size, step))
            step *= 2
    return value


def halve_and_gather(rows, blocks, rounds):
    for axis, size in rounds:
        step = 1
        while step < size:
            pairs = partners(size, step)
            half = rows.shape[0] // 2
            upper = (lax.axis_index(axis) // step) % 2 == 1
            low, high = rows[:half], rows[half:]
            keep = jnp.where(upper, high, low)
            give = jnp.where(upper, low, high)
            rows = keep + lax.ppermute(give, axis, pairs)
            blocks = jnp.concatenate([blocks, lax.ppermute(blocks, axis, pairs)], axis=0)
            rows, blocks = lax.optimization_barrier((rows, blocks))
            step *= 2
    return rows, blocks


def on_device(soc_ints, cou_ints, coef_t, active_rdm, spin_dens, pair_list, owner_map, state_count):
    width = coef_t.shape[0]
    cells = width * width
    rows = soc_ints.shape[0]
    n_aux = lax.axis_size("z") * lax.axis_size("xlo")
    scale = 1.0 / (8.0 * jnp.sqrt(jnp.float32(rows * n_aux)))

    soc_part = jnp.einsum(
        "pkn,vn->pkv", soc_ints.reshape(rows, 3 * width, -1), coef_t, preferred_element_type=jnp.float32
    ).reshape(rows, 3 * cells)
    cou_part = jnp.einsum("ptn,un->ptu", cou_ints, coef_t, preferred_element_type=jnp.float32)
    fitted = jnp.einsum("ptu,tu->p", cou_part, active_rdm, precision=HIGH)
    folded = jnp.einsum("vw,pwu->pvu", active_rdm, cou_part, precision=HIGH)
    eye = jnp.eye(width, dtype=jnp.float32)
    weight = (fitted[:, None, None] * eye[None] - 1.5 * folded).reshape(rows, cells)

    joined = jnp.concatenate([soc_part, weight], axis=1)
    share, every_dens = halve_and_gather(joined, spin_dens, AO_ROUNDS)
    count = share.shape[0]
    soc_mo = share[:, : 3 * cells].reshape(count, 3, width, width)
    weight = share[:, 3 * cells :].reshape(count, width, width)
    field_part = jnp.einsum("pxtv,pvu->xtu", soc_mo, weight, precision=HIGH) * scale
    field = butterfly_sum(field_part.reshape(3, cells), AO_ROUNDS + AUX_ROUNDS)

    me = (lax.axis_index("y") * 4 + lax.axis_index("xhi") * 2 + lax.axis_index("core")).astype(jnp.int32)
    block = spin_dens.shape[0]
    where = (owner_map // block) ^ me
    picked = jnp.take(every_dens, where * block + owner_map % block, axis=0)

    bra = jnp.take(state_count, jnp.take(pair_list[:, 0], owner_map, axis=0), axis=0)
    ket = jnp.take(state_count, jnp.take(pair_list[:, 1], owner_map, axis=0), axis=0)
    live = jnp.minimum(bra, ket)
    cell = jnp.arange(cells, dtype=jnp.int32)
    inside = (cell[None, :] // width < live[:, None]) & (cell[None, :] % width < live[:, None])
    dens = jnp.where(inside, picked.astype(jnp.float32), jnp.float32(0.0))
    return jnp.dot(field, dens.T, precision=HIGH) / width


def solution(mesh):
    devices = np.asarray(mesh.devices).reshape(8, 2, 8, 2, 2)
    fine = Mesh(devices, AUX + AO)
    return jax.shard_map(
        on_device,
        mesh=fine,
        in_specs=(
            P(AUX, None, None, AO),
            P(AUX, None, AO),
            P(None, AO),
            P(),
            P(AO, None),
            P(),
            P(AO),
            P(),
        ),
        out_specs=P(None, AO),
        check_vma=False,
    )
```

```python
import jax
import jax.numpy as jnp
import numpy as np
from jax import lax
from jax.sharding import Mesh
from jax.sharding import PartitionSpec as P

AUX = ("z", "xlo")
AO = ("y", "xhi", "core")
HIGH = lax.Precision.HIGHEST
AO_ROUNDS = (("core", 2), ("xhi", 2), ("y", 8))
AUX_ROUNDS = (("xlo", 2), ("z", 8))


def ring_label(position, size):
    if size < 8:
        return position
    return position if position < size // 2 else 3 * size // 2 - 1 - position


def partners(size, step):
    labels = [ring_label(i, size) for i in range(size)]
    return [(i, labels.index(labels[i] ^ step)) for i in range(size)]


def butterfly_sum(value, rounds):
    for axis, size in rounds:
        step = 1
        while step < size:
            value = value + lax.ppermute(value, axis, partners(size, step))
            step *= 2
    return value


def butterfly_sum_gather(total, blocks, rounds):
    for axis, size in rounds:
        step = 1
        while step < size:
            pairs = partners(size, step)
            total = total + lax.ppermute(total, axis, pairs)
            blocks = jnp.concatenate([blocks, lax.ppermute(blocks, axis, pairs)], axis=0)
            total, blocks = lax.optimization_barrier((total, blocks))
            step *= 2
    return total, blocks


def on_device(soc_ints, cou_ints, coef_t, active_rdm, spin_dens, pair_list, owner_map, state_count):
    width = coef_t.shape[0]
    cells = width * width
    rows = soc_ints.shape[0]
    n_aux = lax.axis_size("z") * lax.axis_size("xlo")
    scale = 1.0 / (8.0 * jnp.sqrt(jnp.float32(rows * n_aux)))

    cou_part = jnp.einsum("un,ptn->upt", coef_t, cou_ints, preferred_element_type=jnp.float32)
    fitted = jnp.einsum("upt,tu->p", cou_part, active_rdm, precision=HIGH)
    folded = jnp.einsum("upw,vw->uvp", cou_part, active_rdm, precision=HIGH)
    eye = jnp.eye(width, dtype=jnp.float32)
    weight = (eye[:, :, None] * fitted[None, None, :] - 1.5 * folded).reshape(width, width * rows)
    weight, every_dens = butterfly_sum_gather(weight, spin_dens, AO_ROUNDS)

    soc_part = jnp.einsum(
        "vn,pkn->vpk", coef_t, soc_ints.reshape(rows, 3 * width, -1), preferred_element_type=jnp.float32
    ).reshape(width * rows, 3 * width)
    field_part = jnp.dot(weight, soc_part, precision=HIGH) * scale
    field = butterfly_sum(field_part, AO_ROUNDS + AUX_ROUNDS)

    def labelled(device):
        y = device // 4
        return jnp.where(y < 4, y, 11 - y) * 4 + device % 4

    me = (lax.axis_index("y") * 4 + lax.axis_index("xhi") * 2 + lax.axis_index("core")).astype(jnp.int32)
    block = spin_dens.shape[0]
    where = labelled(owner_map // block) ^ labelled(me)
    picked = jnp.take(every_dens, where * block + owner_map % block, axis=0)

    bra = jnp.take(state_count, jnp.take(pair_list[:, 0], owner_map, axis=0), axis=0)
    ket = jnp.take(state_count, jnp.take(pair_list[:, 1], owner_map, axis=0), axis=0)
    live = jnp.minimum(bra, ket)
    cell = jnp.arange(cells, dtype=jnp.int32)
    inside = (cell[None, :] // width < live[:, None]) & (cell[None, :] % width < live[:, None])
    dens = jnp.where(inside, picked.astype(jnp.float32), jnp.float32(0.0))
    return jnp.einsum(
        "uxt,stu->xs", field.reshape(width, 3, width), dens.reshape(-1, width, width), precision=HIGH
    ) / width


def solution(mesh):
    devices = np.asarray(mesh.devices).reshape(8, 2, 8, 2, 2)
    fine = Mesh(devices, AUX + AO)
    return jax.shard_map(
        on_device,
        mesh=fine,
        in_specs=(
            P(AUX, None, None, AO),
            P(AUX, None, AO),
            P(None, AO),
            P(),
            P(AO, None),
            P(),
            P(AO),
            P(),
        ),
        out_specs=P(None, AO),
        check_vma=False,
    )
```

```python
import jax
import jax.numpy as jnp
import numpy as np
from jax import lax
from jax.sharding import Mesh
from jax.sharding import PartitionSpec as P

AUX = ("z", "xlo")
AO = ("y", "xhi", "core")
HIGH = lax.Precision.HIGHEST
AO_ROUNDS = (("core", 2), ("xhi", 2), ("y", 8))
AUX_ROUNDS = (("xlo", 2), ("z", 8))


def ring_label(position, size):
    if size != 8:
        return position
    return position if position < 4 else position ^ 2


def partners(size, step):
    labels = [ring_label(i, size) for i in range(size)]
    return [(i, labels.index(labels[i] ^ step)) for i in range(size)]


def butterfly_sum(value, rounds):
    for axis, size in rounds:
        step = 1
        while step < size:
            value = value + lax.ppermute(value, axis, partners(size, step))
            step *= 2
    return value


def x_ring_sum(value):
    for pairs in ([(i, i ^ 2) for i in range(4)], [(i, 3 - i) for i in range(4)]):
        value = value + lax.ppermute(value, ("xlo", "xhi"), pairs)
    return value


def butterfly_sum_gather(total, blocks, rounds):
    for axis, size in rounds:
        step = 1
        while step < size:
            pairs = partners(size, step)
            total = total + lax.ppermute(total, axis, pairs)
            blocks = jnp.concatenate([blocks, lax.ppermute(blocks, axis, pairs)], axis=0)
            total, blocks = lax.optimization_barrier((total, blocks))
            step *= 2
    return total, blocks


def on_device(soc_ints, cou_ints, coef_t, active_rdm, spin_dens, pair_list, owner_map, state_count):
    width = coef_t.shape[0]
    cells = width * width
    rows = soc_ints.shape[0]
    n_aux = lax.axis_size("z") * lax.axis_size("xlo")
    scale = 1.0 / (8.0 * jnp.sqrt(jnp.float32(rows * n_aux)))

    cou_part = jnp.einsum("un,ptn->upt", coef_t, cou_ints, preferred_element_type=jnp.float32)
    fitted = jnp.einsum("upt,tu->p", cou_part, active_rdm, precision=HIGH)
    folded = jnp.einsum("upw,vw->uvp", cou_part, active_rdm, precision=HIGH)
    eye = jnp.eye(width, dtype=jnp.float32)
    weight = (eye[:, :, None] * fitted[None, None, :] - 1.5 * folded).reshape(width, width * rows)
    weight, every_dens = butterfly_sum_gather(weight, spin_dens, AO_ROUNDS)

    soc_part = jnp.einsum(
        "vn,pkn->vpk", coef_t, soc_ints.reshape(rows, 3 * width, -1), preferred_element_type=jnp.float32
    ).reshape(width * rows, 3 * width)
    field_part = jnp.dot(weight, soc_part, precision=HIGH) * scale
    field = butterfly_sum(field_part, (("core", 2),))
    field = x_ring_sum(field)
    field = butterfly_sum(field, (("y", 8), ("z", 8)))

    def labelled(device):
        y = device // 4
        return jnp.where(y < 4, y, y ^ 2) * 4 + device % 4

    me = (lax.axis_index("y") * 4 + lax.axis_index("xhi") * 2 + lax.axis_index("core")).astype(jnp.int32)
    block = spin_dens.shape[0]
    where = labelled(owner_map // block) ^ labelled(me)
    picked = jnp.take(every_dens, where * block + owner_map % block, axis=0)

    bra = jnp.take(state_count, jnp.take(pair_list[:, 0], owner_map, axis=0), axis=0)
    ket = jnp.take(state_count, jnp.take(pair_list[:, 1], owner_map, axis=0), axis=0)
    live = jnp.minimum(bra, ket)
    cell = jnp.arange(cells, dtype=jnp.int32)
    inside = (cell[None, :] // width < live[:, None]) & (cell[None, :] % width < live[:, None])
    dens = jnp.where(inside, picked.astype(jnp.float32), jnp.float32(0.0))
    return jnp.einsum(
        "uxt,stu->xs", field.reshape(width, 3, width), dens.reshape(-1, width, width), precision=HIGH
    ) / width


def solution(mesh):
    devices = np.asarray(mesh.devices).reshape(8, 2, 8, 2, 2)
    fine = Mesh(devices, AUX + AO)
    return jax.shard_map(
        on_device,
        mesh=fine,
        in_specs=(
            P(AUX, None, None, AO),
            P(AUX, None, AO),
            P(None, AO),
            P(),
            P(AO, None),
            P(),
            P(AO),
            P(),
        ),
        out_specs=P(None, AO),
        check_vma=False,
    )
```

```python
import jax
import jax.numpy as jnp
import numpy as np
from jax import lax
from jax.sharding import Mesh
from jax.sharding import PartitionSpec as P

AUX = ("z", "xlo")
AO = ("y", "xhi", "core")
HIGH = lax.Precision.HIGHEST
AO_ROUNDS = (("core", 2), ("xhi", 2), ("y", 8))
AUX_ROUNDS = (("xlo", 2), ("z", 8))


def ring_label(position, size):
    if size != 8:
        return position
    return position if position < 4 else position ^ 2


def partners(size, step):
    labels = [ring_label(i, size) for i in range(size)]
    return [(i, labels.index(labels[i] ^ step)) for i in range(size)]


def butterfly_sum(value, rounds):
    for axis, size in rounds:
        step = 1
        while step < size:
            value = value + lax.ppermute(value, axis, partners(size, step))
            step *= 2
    return value


def x_ring_sum(value):
    for pairs in ([(i, i ^ 2) for i in range(4)], [(i, 3 - i) for i in range(4)]):
        value = value + lax.ppermute(value, ("xlo", "xhi"), pairs)
    return value


def butterfly_sum_gather(total, blocks, rounds):
    for axis, size in rounds:
        step = 1
        while step < size:
            pairs = partners(size, step)
            total = total + lax.ppermute(total, axis, pairs)
            blocks = jnp.concatenate([blocks, lax.ppermute(blocks, axis, pairs)], axis=0)
            total, blocks = lax.optimization_barrier((total, blocks))
            step *= 2
    return total, blocks


def on_device(soc_ints, cou_ints, coef_t, active_rdm, spin_dens, pair_list, owner_map, state_count):
    width = coef_t.shape[0]
    cells = width * width
    rows = soc_ints.shape[0]
    n_aux = lax.axis_size("z") * lax.axis_size("xlo")
    scale = 1.0 / (8.0 * jnp.sqrt(jnp.float32(rows * n_aux)))

    cou_part = jnp.einsum("un,ptn->upt", coef_t, cou_ints, preferred_element_type=jnp.float32)
    fitted = jnp.einsum("upt,tu->p", cou_part, active_rdm, precision=HIGH)
    folded = jnp.einsum("upw,vw->uvp", cou_part, active_rdm, precision=HIGH)
    eye = jnp.eye(width, dtype=jnp.float32)
    weight = (eye[:, :, None] * fitted[None, None, :] - 1.5 * folded).reshape(width, width * rows)
    weight, every_dens = butterfly_sum_gather(weight, spin_dens, (("y", 8), ("xhi", 2), ("core", 2)))

    soc_part = jnp.einsum(
        "vn,pkn->vpk", coef_t, soc_ints.reshape(rows, 3 * width, -1), preferred_element_type=jnp.float32
    ).reshape(width * rows, 3 * width)
    field_part = jnp.dot(weight, soc_part, precision=HIGH) * scale
    field = butterfly_sum(field_part, (("core", 2),))
    field = x_ring_sum(field)
    field = butterfly_sum(field, (("y", 8), ("z", 8)))

    def labelled(device):
        y = device // 4
        return (device % 2) * 16 + (device // 2 % 2) * 8 + jnp.where(y < 4, y, y ^ 2)

    me = (lax.axis_index("y") * 4 + lax.axis_index("xhi") * 2 + lax.axis_index("core")).astype(jnp.int32)
    block = spin_dens.shape[0]
    where = labelled(owner_map // block) ^ labelled(me)
    picked = jnp.take(every_dens, where * block + owner_map % block, axis=0)

    bra = jnp.take(state_count, jnp.take(pair_list[:, 0], owner_map, axis=0), axis=0)
    ket = jnp.take(state_count, jnp.take(pair_list[:, 1], owner_map, axis=0), axis=0)
    live = jnp.minimum(bra, ket)
    cell = jnp.arange(cells, dtype=jnp.int32)
    inside = (cell[None, :] // width < live[:, None]) & (cell[None, :] % width < live[:, None])
    dens = jnp.where(inside, picked.astype(jnp.float32), jnp.float32(0.0))
    return jnp.einsum(
        "uxt,stu->xs", field.reshape(width, 3, width), dens.reshape(-1, width, width), precision=HIGH
    ) / width


def solution(mesh):
    devices = np.asarray(mesh.devices).reshape(8, 2, 8, 2, 2)
    fine = Mesh(devices, AUX + AO)
    return jax.shard_map(
        on_device,
        mesh=fine,
        in_specs=(
            P(AUX, None, None, AO),
            P(AUX, None, AO),
            P(None, AO),
            P(),
            P(AO, None),
            P(),
            P(AO),
            P(),
        ),
        out_specs=P(None, AO),
        check_vma=False,
    )
```

```python
import jax
import jax.numpy as jnp
import numpy as np
from jax import lax
from jax.sharding import Mesh
from jax.sharding import PartitionSpec as P

AUX = ("z", "xlo")
AO = ("y", "xhi", "core")
HIGH = lax.Precision.HIGHEST
AO_ROUNDS = (("core", 2), ("xhi", 2), ("y", 8))
AUX_ROUNDS = (("xlo", 2), ("z", 8))


def ring_label(position, size):
    if size != 8:
        return position
    return position if position < 4 else position ^ 2


def partners(size, step):
    labels = [ring_label(i, size) for i in range(size)]
    return [(i, labels.index(labels[i] ^ step)) for i in range(size)]


def butterfly_sum(value, rounds):
    for axis, size in rounds:
        step = 1
        while step < size:
            value = value + lax.ppermute(value, axis, partners(size, step))
            step *= 2
    return value


def x_ring_sum(value):
    for pairs in ([(i, i ^ 2) for i in range(4)], [(i, 3 - i) for i in range(4)]):
        value = value + lax.ppermute(value, ("xlo", "xhi"), pairs)
    return value


def butterfly_sum_gather(total, blocks, rounds):
    for axis, size in rounds:
        step = 1
        while step < size:
            pairs = partners(size, step)
            total = total + lax.ppermute(total, axis, pairs)
            blocks = jnp.concatenate([blocks, lax.ppermute(blocks, axis, pairs)], axis=0)
            total, blocks = lax.optimization_barrier((total, blocks))
            step *= 2
    return total, blocks


def on_device(soc_ints, cou_ints, coef_t, active_rdm, spin_dens, pair_list, owner_map, state_count):
    width = coef_t.shape[0]
    cells = width * width
    rows = soc_ints.shape[0]
    n_aux = lax.axis_size("z") * lax.axis_size("xlo")
    scale = 1.0 / (8.0 * jnp.sqrt(jnp.float32(rows * n_aux)))

    cou_part = jnp.einsum("un,ptn->upt", coef_t, cou_ints, preferred_element_type=jnp.float32)
    fitted = jnp.einsum("upt,tu->p", cou_part, active_rdm, precision=HIGH)
    folded = jnp.einsum("upw,vw->uvp", cou_part, active_rdm, precision=HIGH)
    eye = jnp.eye(width, dtype=jnp.float32)
    weight = (eye[:, :, None] * fitted[None, None, :] - 1.5 * folded).reshape(width, width * rows)
    weight, every_dens = butterfly_sum_gather(weight, spin_dens, (("y", 8), ("xhi", 2), ("core", 2)))

    soc_part = jnp.einsum(
        "vn,pkn->vpk", coef_t, soc_ints.reshape(rows, 3 * width, -1), preferred_element_type=jnp.float32
    ).reshape(width * rows, 3 * width)
    field_part = jnp.dot(weight, soc_part, precision=HIGH) * scale
    field = butterfly_sum(field_part, (("z", 8), ("y", 8)))
    field = x_ring_sum(field)
    field = butterfly_sum(field, (("core", 2),))

    def labelled(device):
        y = device // 4
        return (device % 2) * 16 + (device // 2 % 2) * 8 + jnp.where(y < 4, y, y ^ 2)

    me = (lax.axis_index("y") * 4 + lax.axis_index("xhi") * 2 + lax.axis_index("core")).astype(jnp.int32)
    block = spin_dens.shape[0]
    where = labelled(owner_map // block) ^ labelled(me)
    picked = jnp.take(every_dens, where * block + owner_map % block, axis=0)

    bra = jnp.take(state_count, jnp.take(pair_list[:, 0], owner_map, axis=0), axis=0)
    ket = jnp.take(state_count, jnp.take(pair_list[:, 1], owner_map, axis=0), axis=0)
    live = jnp.minimum(bra, ket)
    cell = jnp.arange(cells, dtype=jnp.int32)
    inside = (cell[None, :] // width < live[:, None]) & (cell[None, :] % width < live[:, None])
    dens = jnp.where(inside, picked.astype(jnp.float32), jnp.float32(0.0))
    return jnp.einsum(
        "uxt,stu->xs", field.reshape(width, 3, width), dens.reshape(-1, width, width), precision=HIGH
    ) / width


def solution(mesh):
    devices = np.asarray(mesh.devices).reshape(8, 2, 8, 2, 2)
    fine = Mesh(devices, AUX + AO)
    return jax.shard_map(
        on_device,
        mesh=fine,
        in_specs=(
            P(AUX, None, None, AO),
            P(AUX, None, AO),
            P(None, AO),
            P(),
            P(AO, None),
            P(),
            P(AO),
            P(),
        ),
        out_specs=P(None, AO),
        check_vma=False,
    )
```

```python
import jax
import jax.numpy as jnp
import numpy as np
from jax import lax
from jax.sharding import Mesh
from jax.sharding import PartitionSpec as P

AUX = ("z", "xlo")
AO = ("y", "xhi", "core")
HIGH = lax.Precision.HIGHEST
AO_ROUNDS = (("core", 2), ("xhi", 2), ("y", 8))
AUX_ROUNDS = (("xlo", 2), ("z", 8))


def ring_label(position, size):
    if size != 8:
        return position
    return position if position < 4 else position ^ 2


def partners(size, step):
    labels = [ring_label(i, size) for i in range(size)]
    return [(i, labels.index(labels[i] ^ step)) for i in range(size)]


def butterfly_sum(value, rounds):
    for axis, size in rounds:
        step = 1
        while step < size:
            value = value + lax.ppermute(value, axis, partners(size, step))
            step *= 2
    return value


def x_ring_sum(value):
    for pairs in ([(i, i ^ 2) for i in range(4)], [(i, 3 - i) for i in range(4)]):
        value = value + lax.ppermute(value, ("xlo", "xhi"), pairs)
    return value


def steps_of(rounds):
    return [(axis, size, 1 << k) for axis, size in rounds for k in range(size.bit_length() - 1)]


def gather_round(blocks, step):
    axis, size, distance = step
    return jnp.concatenate([blocks, lax.ppermute(blocks, axis, partners(size, distance))], axis=0)


def butterfly_sum_gather(total, blocks, steps):
    for i, (axis, size, distance) in enumerate(steps):
        total = total + lax.ppermute(total, axis, partners(size, distance))
        if i + 1 < len(steps):
            blocks = gather_round(blocks, steps[i + 1])
        total, blocks = lax.optimization_barrier((total, blocks))
    return total, blocks


def on_device(soc_ints, cou_ints, coef_t, active_rdm, spin_dens, pair_list, owner_map, state_count):
    width = coef_t.shape[0]
    cells = width * width
    rows = soc_ints.shape[0]
    n_aux = lax.axis_size("z") * lax.axis_size("xlo")
    scale = 1.0 / (8.0 * jnp.sqrt(jnp.float32(rows * n_aux)))

    steps = steps_of((("y", 8), ("xhi", 2), ("core", 2)))
    first = gather_round(spin_dens, steps[0])
    cou_part = jnp.einsum("un,ptn->upt", coef_t, cou_ints, preferred_element_type=jnp.float32)
    cou_part, first = lax.optimization_barrier((cou_part, first))
    fitted = jnp.einsum("upt,tu->p", cou_part, active_rdm, precision=HIGH)
    folded = jnp.einsum("upw,vw->uvp", cou_part, active_rdm, precision=HIGH)
    eye = jnp.eye(width, dtype=jnp.float32)
    weight = (eye[:, :, None] * fitted[None, None, :] - 1.5 * folded).reshape(width, width * rows)
    weight, every_dens = butterfly_sum_gather(weight, first, steps)

    soc_part = jnp.einsum(
        "vn,pkn->vpk", coef_t, soc_ints.reshape(rows, 3 * width, -1), preferred_element_type=jnp.float32
    ).reshape(width * rows, 3 * width)
    field_part = jnp.dot(weight, soc_part, precision=HIGH) * scale
    field = butterfly_sum(field_part, (("core", 2),))
    field = x_ring_sum(field)
    field = butterfly_sum(field, (("y", 8), ("z", 8)))

    def labelled(device):
        y = device // 4
        return (device % 2) * 16 + (device // 2 % 2) * 8 + jnp.where(y < 4, y, y ^ 2)

    me = (lax.axis_index("y") * 4 + lax.axis_index("xhi") * 2 + lax.axis_index("core")).astype(jnp.int32)
    block = spin_dens.shape[0]
    where = labelled(owner_map // block) ^ labelled(me)
    picked = jnp.take(every_dens, where * block + owner_map % block, axis=0)

    bra = jnp.take(state_count, jnp.take(pair_list[:, 0], owner_map, axis=0), axis=0)
    ket = jnp.take(state_count, jnp.take(pair_list[:, 1], owner_map, axis=0), axis=0)
    live = jnp.minimum(bra, ket)
    cell = jnp.arange(cells, dtype=jnp.int32)
    inside = (cell[None, :] // width < live[:, None]) & (cell[None, :] % width < live[:, None])
    dens = jnp.where(inside, picked.astype(jnp.float32), jnp.float32(0.0))
    return jnp.einsum(
        "uxt,stu->xs", field.reshape(width, 3, width), dens.reshape(-1, width, width), precision=HIGH
    ) / width


def solution(mesh):
    devices = np.asarray(mesh.devices).reshape(8, 2, 8, 2, 2)
    fine = Mesh(devices, AUX + AO)
    return jax.shard_map(
        on_device,
        mesh=fine,
        in_specs=(
            P(AUX, None, None, AO),
            P(AUX, None, AO),
            P(None, AO),
            P(),
            P(AO, None),
            P(),
            P(AO),
            P(),
        ),
        out_specs=P(None, AO),
        check_vma=False,
    )
```

```python
import jax
import jax.numpy as jnp
import numpy as np
from jax import lax
from jax.sharding import Mesh
from jax.sharding import PartitionSpec as P

AUX = ("z", "xlo")
AO = ("y", "xhi", "core")
HIGH = lax.Precision.HIGHEST
AO_ROUNDS = (("core", 2), ("xhi", 2), ("y", 8))
AUX_ROUNDS = (("xlo", 2), ("z", 8))


def ring_label(position, size):
    if size != 8:
        return position
    return position if position < 4 else position ^ 2


def partners(size, step):
    labels = [ring_label(i, size) for i in range(size)]
    return [(i, labels.index(labels[i] ^ step)) for i in range(size)]


def butterfly_sum(value, rounds):
    for axis, size in rounds:
        step = 1
        while step < size:
            value = value + lax.ppermute(value, axis, partners(size, step))
            step *= 2
    return value


def x_ring_sum(value):
    for pairs in ([(i, i ^ 2) for i in range(4)], [(i, 3 - i) for i in range(4)]):
        value = value + lax.ppermute(value, ("xlo", "xhi"), pairs)
    return value


def butterfly_sum_gather(total, blocks, rounds):
    for axis, size in rounds:
        step = 1
        while step < size:
            pairs = partners(size, step)
            total = total + lax.ppermute(total, axis, pairs)
            blocks = jnp.concatenate([blocks, lax.ppermute(blocks, axis, pairs)], axis=0)
            total, blocks = lax.optimization_barrier((total, blocks))
            step *= 2
    return total, blocks


def on_device(soc_ints, cou_ints, coef_t, active_rdm, spin_dens, pair_list, owner_map, state_count):
    width = coef_t.shape[0]
    cells = width * width
    rows = soc_ints.shape[0]
    n_aux = lax.axis_size("z") * lax.axis_size("xlo")
    scale = 1.0 / (8.0 * jnp.sqrt(jnp.float32(rows * n_aux)))

    cou_part = jnp.einsum("un,ptn->upt", coef_t, cou_ints, preferred_element_type=jnp.float32)
    eye = jnp.eye(width, dtype=jnp.float32)
    table = jnp.einsum("ta,uv->atuv", active_rdm, eye) - 1.5 * jnp.einsum("vt,au->atuv", active_rdm, eye)
    weight = jnp.einsum("apt,atuv->uvp", cou_part, table, precision=HIGH).reshape(width, width * rows)
    weight, every_dens = butterfly_sum_gather(weight, spin_dens, (("y", 8), ("xhi", 2), ("core", 2)))

    soc_part = jnp.einsum(
        "vn,pkn->vpk", coef_t, soc_ints.reshape(rows, 3 * width, -1), preferred_element_type=jnp.float32
    ).reshape(width * rows, 3 * width)
    field_part = jnp.dot(weight, soc_part, precision=HIGH) * scale
    field = butterfly_sum(field_part, (("core", 2),))
    field = x_ring_sum(field)
    field = butterfly_sum(field, (("y", 8), ("z", 8)))

    def labelled(device):
        y = device // 4
        return (device % 2) * 16 + (device // 2 % 2) * 8 + jnp.where(y < 4, y, y ^ 2)

    me = (lax.axis_index("y") * 4 + lax.axis_index("xhi") * 2 + lax.axis_index("core")).astype(jnp.int32)
    block = spin_dens.shape[0]
    where = labelled(owner_map // block) ^ labelled(me)
    picked = jnp.take(every_dens, where * block + owner_map % block, axis=0)

    bra = jnp.take(state_count, jnp.take(pair_list[:, 0], owner_map, axis=0), axis=0)
    ket = jnp.take(state_count, jnp.take(pair_list[:, 1], owner_map, axis=0), axis=0)
    live = jnp.minimum(bra, ket)
    cell = jnp.arange(cells, dtype=jnp.int32)
    inside = (cell[None, :] // width < live[:, None]) & (cell[None, :] % width < live[:, None])
    dens = jnp.where(inside, picked.astype(jnp.float32), jnp.float32(0.0))
    return jnp.einsum(
        "uxt,stu->xs", field.reshape(width, 3, width), dens.reshape(-1, width, width), precision=HIGH
    ) / width


def solution(mesh):
    devices = np.asarray(mesh.devices).reshape(8, 2, 8, 2, 2)
    fine = Mesh(devices, AUX + AO)
    return jax.shard_map(
        on_device,
        mesh=fine,
        in_specs=(
            P(AUX, None, None, AO),
            P(AUX, None, AO),
            P(None, AO),
            P(),
            P(AO, None),
            P(),
            P(AO),
            P(),
        ),
        out_specs=P(None, AO),
        check_vma=False,
    )
```

```python
import jax
import jax.numpy as jnp
import numpy as np
from jax import lax
from jax.sharding import Mesh
from jax.sharding import PartitionSpec as P

AUX = ("z", "xlo")
AO = ("y", "xhi", "core")
HIGH = lax.Precision.HIGHEST
AO_ROUNDS = (("core", 2), ("xhi", 2), ("y", 8))
AUX_ROUNDS = (("xlo", 2), ("z", 8))


def ring_label(position, size):
    if size != 8:
        return position
    return position if position < 4 else position ^ 2


def partners(size, step):
    labels = [ring_label(i, size) for i in range(size)]
    return [(i, labels.index(labels[i] ^ step)) for i in range(size)]


def butterfly_sum(value, rounds):
    for axis, size in rounds:
        step = 1
        while step < size:
            value = value + lax.ppermute(value, axis, partners(size, step))
            step *= 2
    return value


def x_ring_sum(value):
    for pairs in ([(i, i ^ 2) for i in range(4)], [(i, 3 - i) for i in range(4)]):
        value = value + lax.ppermute(value, ("xlo", "xhi"), pairs)
    return value


def butterfly_sum_gather(total, blocks, rounds):
    for axis, size in rounds:
        step = 1
        while step < size:
            pairs = partners(size, step)
            total = total + lax.ppermute(total, axis, pairs)
            blocks = jnp.concatenate([blocks, lax.ppermute(blocks, axis, pairs)], axis=0)
            total, blocks = lax.optimization_barrier((total, blocks))
            step *= 2
    return total, blocks


def on_device(soc_ints, cou_ints, coef_t, active_rdm, spin_dens, pair_list, owner_map, state_count):
    width = coef_t.shape[0]
    cells = width * width
    rows = soc_ints.shape[0]
    n_aux = lax.axis_size("z") * lax.axis_size("xlo")
    scale = 1.0 / (8.0 * jnp.sqrt(jnp.float32(rows * n_aux)))

    cou_part = jnp.einsum("un,ptn->upt", coef_t, cou_ints, preferred_element_type=jnp.float32)
    fitted = jnp.einsum("upt,tu->p", cou_part, active_rdm, precision=HIGH)
    folded = jnp.einsum("upw,vw->uvp", cou_part, active_rdm, precision=HIGH)
    eye = jnp.eye(width, dtype=jnp.float32)
    weight = (eye[:, :, None] * fitted[None, None, :] - 1.5 * folded).reshape(width, width * rows)
    weight, every_dens = butterfly_sum_gather(weight, spin_dens, (("xhi", 2), ("y", 8), ("core", 2)))

    soc_part = jnp.einsum(
        "vn,pkn->vpk", coef_t, soc_ints.reshape(rows, 3 * width, -1), preferred_element_type=jnp.float32
    ).reshape(width * rows, 3 * width)
    field_part = jnp.dot(weight, soc_part, precision=HIGH) * scale
    field = butterfly_sum(field_part, (("core", 2),))
    field = x_ring_sum(field)
    field = butterfly_sum(field, (("y", 8), ("z", 8)))

    def labelled(device):
        y = device // 4
        return (device % 2) * 16 + jnp.where(y < 4, y, y ^ 2) * 2 + device // 2 % 2

    me = (lax.axis_index("y") * 4 + lax.axis_index("xhi") * 2 + lax.axis_index("core")).astype(jnp.int32)
    block = spin_dens.shape[0]
    where = labelled(owner_map // block) ^ labelled(me)
    picked = jnp.take(every_dens, where * block + owner_map % block, axis=0)

    bra = jnp.take(state_count, jnp.take(pair_list[:, 0], owner_map, axis=0), axis=0)
    ket = jnp.take(state_count, jnp.take(pair_list[:, 1], owner_map, axis=0), axis=0)
    live = jnp.minimum(bra, ket)
    cell = jnp.arange(cells, dtype=jnp.int32)
    inside = (cell[None, :] // width < live[:, None]) & (cell[None, :] % width < live[:, None])
    dens = jnp.where(inside, picked.astype(jnp.float32), jnp.float32(0.0))
    return jnp.einsum(
        "uxt,stu->xs", field.reshape(width, 3, width), dens.reshape(-1, width, width), precision=HIGH
    ) / width


def solution(mesh):
    devices = np.asarray(mesh.devices).reshape(8, 2, 8, 2, 2)
    fine = Mesh(devices, AUX + AO)
    return jax.shard_map(
        on_device,
        mesh=fine,
        in_specs=(
            P(AUX, None, None, AO),
            P(AUX, None, AO),
            P(None, AO),
            P(),
            P(AO, None),
            P(),
            P(AO),
            P(),
        ),
        out_specs=P(None, AO),
        check_vma=False,
    )
```

```python
import jax
import jax.numpy as jnp
import numpy as np
from jax import lax
from jax.sharding import Mesh
from jax.sharding import PartitionSpec as P

AUX = ("z", "xlo")
AO = ("y", "xhi", "core")
HIGH = lax.Precision.HIGHEST
AO_ROUNDS = (("core", 2), ("xhi", 2), ("y", 8))
AUX_ROUNDS = (("xlo", 2), ("z", 8))


def ring_label(position, size):
    if size != 8:
        return position
    return position if position < 4 else position ^ 2


def partners(size, step):
    labels = [ring_label(i, size) for i in range(size)]
    return [(i, labels.index(labels[i] ^ step)) for i in range(size)]


def butterfly_sum(value, rounds):
    for axis, size in rounds:
        step = 1
        while step < size:
            value = value + lax.ppermute(value, axis, partners(size, step))
            step *= 2
    return value


def x_ring_sum(value):
    for pairs in ([(i, i ^ 2) for i in range(4)], [(i, 3 - i) for i in range(4)]):
        value = value + lax.ppermute(value, ("xlo", "xhi"), pairs)
    return value


def butterfly_sum_gather(total, blocks, rounds):
    for axis, size in rounds:
        step = 1
        while step < size:
            pairs = partners(size, step)
            total = total + lax.ppermute(total, axis, pairs)
            blocks = jnp.concatenate([blocks, lax.ppermute(blocks, axis, pairs)], axis=0)
            total, blocks = lax.optimization_barrier((total, blocks))
            step *= 2
    return total, blocks


def on_device(soc_ints, cou_ints, coef_t, active_rdm, spin_dens, pair_list, owner_map, state_count):
    width = coef_t.shape[0]
    cells = width * width
    rows = soc_ints.shape[0]
    n_aux = lax.axis_size("z") * lax.axis_size("xlo")
    scale = 1.0 / (8.0 * jnp.sqrt(jnp.float32(rows * n_aux)))

    cou_part = jnp.einsum("un,ptn->upt", coef_t, cou_ints, preferred_element_type=jnp.float32)
    fitted = jnp.einsum("upt,tu->p", cou_part, active_rdm, precision=HIGH)
    folded = jnp.einsum("upw,vw->uvp", cou_part, active_rdm, precision=HIGH)
    eye = jnp.eye(width, dtype=jnp.float32)
    weight = (eye[:, :, None] * fitted[None, None, :] - 1.5 * folded).reshape(width, width * rows)
    weight, every_dens = butterfly_sum_gather(weight, spin_dens, (("y", 8), ("xhi", 2), ("core", 2)))

    soc_part = jnp.einsum(
        "vn,pkn->vpk", coef_t, soc_ints.reshape(rows, 3 * width, -1), preferred_element_type=jnp.float32
    ).reshape(width * rows, 3 * width)
    field_part = jnp.dot(weight, soc_part, precision=HIGH) * scale
    field = butterfly_sum(field_part, (("core", 2),))
    field = x_ring_sum(field)
    field = butterfly_sum(field, (("z", 8), ("y", 8)))

    def labelled(device):
        y = device // 4
        return (device % 2) * 16 + (device // 2 % 2) * 8 + jnp.where(y < 4, y, y ^ 2)

    me = (lax.axis_index("y") * 4 + lax.axis_index("xhi") * 2 + lax.axis_index("core")).astype(jnp.int32)
    block = spin_dens.shape[0]
    where = labelled(owner_map // block) ^ labelled(me)
    picked = jnp.take(every_dens, where * block + owner_map % block, axis=0)

    bra = jnp.take(state_count, jnp.take(pair_list[:, 0], owner_map, axis=0), axis=0)
    ket = jnp.take(state_count, jnp.take(pair_list[:, 1], owner_map, axis=0), axis=0)
    live = jnp.minimum(bra, ket)
    cell = jnp.arange(cells, dtype=jnp.int32)
    inside = (cell[None, :] // width < live[:, None]) & (cell[None, :] % width < live[:, None])
    dens = jnp.where(inside, picked.astype(jnp.float32), jnp.float32(0.0))
    return jnp.einsum(
        "uxt,stu->xs", field.reshape(width, 3, width), dens.reshape(-1, width, width), precision=HIGH
    ) / width


def solution(mesh):
    devices = np.asarray(mesh.devices).reshape(8, 2, 8, 2, 2)
    fine = Mesh(devices, AUX + AO)
    return jax.shard_map(
        on_device,
        mesh=fine,
        in_specs=(
            P(AUX, None, None, AO),
            P(AUX, None, AO),
            P(None, AO),
            P(),
            P(AO, None),
            P(),
            P(AO),
            P(),
        ),
        out_specs=P(None, AO),
        check_vma=False,
    )
```
